256 devices in a mesh: row: 8 (over y, x_lo), col: 32 (over x_hi, z, core).
Axes of the slice: x: 4 (x_hi: 2, x_lo: 2; x = x_hi * 2 + x_lo), y: 4, z: 8, core: 2. Of those that a mesh axis runs over, the one named last changes fastest.
Arguments:
- vectors: bfloat16 [16, 131072], P(None, ('row', 'col')), may hold values from -6 to 6
- blocks: bfloat16 [8, 6144, 128, 128], P('row', 'col'), may hold values from -0.09375 to 0.09375
- row_ptr: int32 [8, 4128], P('row', 'col'), may hold values from 0 to 192, as said below
- col_idx: int32 [8, 6144], P('row', 'col'), may hold values from 0 to 31, as said below
Outputs:
- product: float32 [16, 131072], P(None, ('row', 'col'))
The draws below stay inside these ranges and needn't reach their ends.
Inputs may be any that keep to these rules, and one draw needn't show every extreme that they name: For each tile, row_ptr starts at 0, never falls, and ends at the tile's count of live slots; at least one tile has exactly 192 live slots in every draw, and counts differ strongly from tile to tile. `col_idx`: within each block row of a tile the live slots name strictly rising block columns, so no block position of a tile is stored twice; slots at or past a tile's count hold a valid column and are unused.
All inputs are finite; a program needn't handle non-finite values.
Results may differ from the reference program's by a relative error of at most 0.0003.
Values may be sent and summed in bfloat16 or wider, within the bound.
No kernel may reach another device: no remote copies, remote signals or barrier semaphores. Data moves between devices by JAX's collectives and lax.ppermute only.
A program may use at most 64 MiB of HBM per device.

```python
import jax
import jax.numpy as jnp
from jax import lax

BLOCK = 128
VECTORS = 16
SEG_BLOCKS = 4
CAPACITY = 192
TILE_ROWS = 128
TILE_COLS = 32
ORDER = 131072
SLOTS = 6144
N_ROW = 8
N_COL = 32


def tile_layout(key):
    base = jax.random.fold_in(key, 11)
    tile_count = N_ROW * N_COL
    spots = TILE_ROWS * TILE_COLS
    keys = jax.random.split(base, 3)
    raw_draw = jax.random.randint(keys[0], (tile_count,), 1, CAPACITY + 1)
    counts = jnp.maximum(raw_draw * raw_draw // CAPACITY, 1)
    fullest = jax.random.randint(keys[1], (), 0, tile_count)
    counts = jnp.where(jnp.arange(tile_count) == fullest, CAPACITY, counts)
    perm_keys = jax.random.split(keys[2], tile_count)
    chosen = jax.vmap(lambda one_key: jax.random.permutation(one_key, spots))(perm_keys)[:, :CAPACITY]
    slot_ids = jnp.arange(CAPACITY)
    keyed = jnp.where(slot_ids[None, :] < counts[:, None], chosen, chosen + spots)
    ordered = jnp.sort(keyed, axis=1)
    live_slots = ordered < spots
    position = ordered % spots
    block_rows = position // TILE_COLS
    block_cols = position % TILE_COLS
    edges = jnp.arange(TILE_ROWS + 1)
    below = live_slots[:, :, None] & (block_rows[:, :, None] < edges[None, None, :])
    pointers = jnp.sum(below.astype(jnp.int32), axis=1)
    return (pointers.reshape(N_ROW, N_COL * (TILE_ROWS + 1)).astype(jnp.int32), block_cols.reshape(N_ROW, N_COL * CAPACITY).astype(jnp.int32))


def draw_row_ptr(key, part):
    return tile_layout(key)[0]


def draw_col_idx(key, part):
    return tile_layout(key)[1]


def level_of(rng, shape, pieces, smallest, top_value):
    factor_of, own = 1.0, jax.random.fold_in(rng, 6)
    for dim, blocks in pieces:
        heights = jnp.exp(jax.random.uniform(jax.random.fold_in(own, dim), (blocks,), jnp.float32, smallest / len(pieces), top_value / len(pieces)))
        factor_of = factor_of * jnp.repeat(heights, shape[dim] // blocks).reshape([-1 if axis == dim else 1 for axis in range(len(shape))])
    return factor_of


def scatter_about(own_key, dims, deviation, bound, cuts=(), held_as=jnp.bfloat16):
    entries = jax.random.normal(own_key, dims, jnp.float32) * deviation
    if len(cuts) > 0:
        entries = level_of(own_key, dims, cuts, -0.22, 0.18) * entries
    return jnp.clip(entries, min=-bound, max=bound).astype(held_as)


def setup_inputs(seed: int = 0) -> dict:
    key_list = jax.random.split(jax.random.key(seed), 5)
    return {
        "vectors": scatter_about(key_list[0], (VECTORS, ORDER), 1.0, 6.0, ((1, 256),)),
        "blocks": scatter_about(key_list[1], (N_ROW, SLOTS, BLOCK, BLOCK), (2 * CAPACITY * BLOCK // (3 * SEG_BLOCKS)) ** -0.5, 0.09375, ((0, 8), (1, 32))),
        "row_ptr": draw_row_ptr(jax.random.fold_in(key_list[4], 71), 0),
        "col_idx": draw_col_idx(jax.random.fold_in(key_list[4], 71), 0),
    }


def tile_terms(row_side, col_side, tile_blocks, pointers, columns):
    slot_ids = jnp.arange(tile_blocks.shape[0], dtype=jnp.int32)
    live_slots = slot_ids < pointers[-1]
    slot_rows = jnp.sum((slot_ids[:, None] >= pointers[None, 1:]).astype(jnp.int32), axis=1)
    slot_rows = jnp.minimum(slot_rows, pointers.shape[0] - 2).astype(jnp.int32)
    count_vectors = row_side.shape[0]
    edge = tile_blocks.shape[1]
    row_blocks = row_side.reshape(count_vectors, -1, edge)
    col_blocks = col_side.reshape(count_vectors, -1, edge)
    picked_rows = jnp.take(row_blocks, slot_rows, axis=1).astype(jnp.float32)
    picked_cols = jnp.take(col_blocks, columns, axis=1).astype(jnp.float32)
    widened = tile_blocks.astype(jnp.float32)
    forward = jnp.einsum("ksj,sij->ski", picked_cols, widened)
    backward = jnp.einsum("ksi,sij->skj", picked_rows, widened)
    live_mask = live_slots[:, None, None]
    forward = jnp.where(live_mask, forward, jnp.zeros_like(forward))
    backward = jnp.where(live_mask, backward, jnp.zeros_like(backward))
    forward_sum = jax.ops.segment_sum(forward, slot_rows, num_segments=row_blocks.shape[1])
    backward_sum = jax.ops.segment_sum(backward, columns, num_segments=col_blocks.shape[1])
    return forward_sum, backward_sum


def reference(vectors, blocks, row_ptr, col_idx):
    count_vectors = vectors.shape[0]
    segment = vectors.shape[1] // (N_ROW * N_COL)
    by_segment = vectors.reshape(count_vectors, N_ROW, N_COL, segment)
    tile_blocks = blocks.reshape(N_ROW, N_COL, -1, BLOCK, BLOCK)
    pointers = row_ptr.reshape(N_ROW, N_COL, -1)
    columns = col_idx.reshape(N_ROW, N_COL, -1)

    def advance(carry, index):
        forward_total, backward_total = carry
        row_at = index // N_COL
        col_at = index % N_COL
        row_side = lax.dynamic_index_in_dim(by_segment, row_at, 1, keepdims=False).reshape(count_vectors, -1)
        col_side = lax.dynamic_index_in_dim(by_segment, col_at, 2, keepdims=False).reshape(count_vectors, -1)
        forward_sum, backward_sum = tile_terms(row_side, col_side, tile_blocks[row_at, col_at], pointers[row_at, col_at], columns[row_at, col_at])
        forward_total = forward_total.at[row_at].add(forward_sum)
        backward_total = backward_total.at[col_at].add(backward_sum)
        return (forward_total, backward_total), None

    start = (jnp.zeros((N_ROW, TILE_ROWS, count_vectors, BLOCK), jnp.float32), jnp.zeros((N_COL, TILE_COLS, count_vectors, BLOCK), jnp.float32))
    (forward_total, backward_total), _ = lax.scan(advance, start, jnp.arange(N_ROW * N_COL, dtype=jnp.int32))
    forward_parts = forward_total.reshape(N_ROW * N_COL, SEG_BLOCKS, count_vectors, BLOCK)
    backward_parts = backward_total.reshape(N_COL, N_ROW, SEG_BLOCKS, count_vectors, BLOCK).transpose(1, 0, 2, 3, 4).reshape(N_ROW * N_COL, SEG_BLOCKS, count_vectors, BLOCK)
    combined = forward_parts + backward_parts
    return combined.transpose(2, 0, 1, 3).reshape(count_vectors, -1)
```

```python
import functools

import jax
import jax.numpy as jnp
from jax import lax
from jax.experimental import pallas as pl
from jax.experimental.pallas import tpu as pltpu
from jax.sharding import PartitionSpec as P

GROUP = 16


def _tile_kernel(rows_ref, cols_ref, count_ref, blocks_ref, vec_ref, out_ref, *, forward):
    g = pl.program_id(0)

    @pl.when(g == 0)
    def _():
        out_ref[...] = jnp.zeros_like(out_ref)

    count = count_ref[0]

    def step(t, carry):
        s = g * GROUP + t
        i = rows_ref[s]
        q = cols_ref[s]
        blk = blocks_ref[t]

        @pl.when(s < count)
        def _():
            if forward:
                part = lax.dot_general(
                    vec_ref[q], blk, (((1,), (1,)), ((), ())), preferred_element_type=jnp.float32
                )
                out_ref[i] += part
            else:
                part = jnp.dot(vec_ref[i], blk, preferred_element_type=jnp.float32)
                out_ref[q] += part

        return carry

    lax.fori_loop(0, GROUP, step, 0, unroll=True)


def tile_apply(slot_rows, columns, count, blocks, vec_blocks, out_blocks, forward):
    slots, edge, _ = blocks.shape
    count_vectors = vec_blocks.shape[1]
    kernel = functools.partial(_tile_kernel, forward=forward)
    grid_spec = pltpu.PrefetchScalarGridSpec(
        num_scalar_prefetch=3,
        grid=(slots // GROUP,),
        in_specs=[
            pl.BlockSpec((GROUP, edge, edge), lambda g, *_: (g, 0, 0)),
            pl.BlockSpec(vec_blocks.shape, lambda g, *_: (0, 0, 0)),
        ],
        out_specs=pl.BlockSpec((out_blocks, count_vectors, edge), lambda g, *_: (0, 0, 0)),
    )
    return pl.pallas_call(
        kernel,
        grid_spec=grid_spec,
        out_shape=jax.ShapeDtypeStruct((out_blocks, count_vectors, edge), jnp.float32),
        compiler_params=pltpu.CompilerParams(dimension_semantics=("arbitrary",)),
        cost_estimate=pl.CostEstimate(
            flops=2 * slots * count_vectors * edge * edge,
            transcendentals=0,
            bytes_accessed=slots * edge * edge * 2 + out_blocks * count_vectors * edge * 4,
        ),
    )(slot_rows, columns, count, blocks, vec_blocks)


def body(vectors, blocks, row_ptr, col_idx):
    count_vectors = vectors.shape[0]
    segment = vectors.shape[1]
    tile_blocks = blocks[0]
    slots, edge, _ = tile_blocks.shape
    pointers = row_ptr[0]
    columns = col_idx[0]
    tile_rows = pointers.shape[0] - 1
    seg_blocks = segment // edge
    grid_rows = lax.axis_size("row")
    tile_cols = grid_rows * seg_blocks

    slot_ids = jnp.arange(slots, dtype=jnp.int32)
    slot_rows = jnp.sum((slot_ids[:, None] >= pointers[None, 1:]).astype(jnp.int32), axis=1)
    slot_rows = jnp.minimum(slot_rows, tile_rows - 1).astype(jnp.int32)
    columns = jnp.clip(columns, 0, tile_cols - 1).astype(jnp.int32)
    count = pointers[-1:].astype(jnp.int32)

    own = vectors.reshape(count_vectors, seg_blocks, edge).transpose(1, 0, 2)
    col_side = ag_a2a(own, "row")
    row_side = ag_a2a(own, "col")

    forward_sum = tile_apply(slot_rows, columns, count, tile_blocks, col_side, tile_rows, True)
    forward_part = rs_a2a(forward_sum, "col")
    backward_sum = tile_apply(slot_rows, columns, count, tile_blocks, row_side, tile_cols, False)
    backward_part = rs_a2a(backward_sum, "row")
    combined = forward_part + backward_part
    return combined.transpose(1, 0, 2).reshape(count_vectors, segment)


def solution(mesh):
    in_specs = (
        P(None, ("row", "col")),
        P("row", "col", None, None),
        P("row", "col"),
        P("row", "col"),
    )
    out_specs = P(None, ("row", "col"))
    return jax.shard_map(body, mesh=mesh, in_specs=in_specs, out_specs=out_specs, check_vma=False)


def ag_doubling(x, axis):
    n = lax.axis_size(axis)
    me = lax.axis_index(axis)
    buf = x
    b = 1
    while b < n:
        recv = lax.ppermute(buf, axis, [(i, i ^ b) for i in range(n)])
        low = (me & b) == 0
        buf = jnp.concatenate([jnp.where(low, buf, recv), jnp.where(low, recv, buf)], 0)
        b *= 2
    return buf


def rs_a2a(x, axis):
    n = lax.axis_size(axis)
    y = lax.all_to_all(x, axis, 0, 0, tiled=True)
    return y.reshape(n, -1, *x.shape[1:]).sum(0)


def ag_a2a(x, axis):
    n = lax.axis_size(axis)
    y = jnp.broadcast_to(x[None], (n,) + x.shape).reshape(n * x.shape[0], *x.shape[1:])
    return lax.all_to_all(y, axis, 0, 0, tiled=True)
```

```python
import functools

import jax
import jax.numpy as jnp
from jax import lax
from jax.experimental import pallas as pl
from jax.experimental.pallas import tpu as pltpu
from jax.sharding import PartitionSpec as P

GROUP = 16


def _tile_kernel(rows_ref, cols_ref, count_ref, blocks_ref, vec_ref, out_ref, *, forward):
    g = pl.program_id(0)

    @pl.when(g == 0)
    def _():
        out_ref[...] = jnp.zeros_like(out_ref)

    count = count_ref[0]
    parts = []
    for t in range(GROUP):
        s = g * GROUP + t
        blk = blocks_ref[t]
        if forward:
            part = lax.dot_general(
                vec_ref[cols_ref[s]], blk, (((1,), (1,)), ((), ())),
                preferred_element_type=jnp.float32,
            )
        else:
            part = jnp.dot(vec_ref[rows_ref[s]], blk, preferred_element_type=jnp.float32)
        parts.append(jnp.where(s < count, part, jnp.zeros_like(part)))
    for t in range(GROUP):
        s = g * GROUP + t
        target = rows_ref[s] if forward else cols_ref[s]
        out_ref[target] += parts[t]


def tile_apply(slot_rows, columns, count, blocks, vec_blocks, out_blocks, forward):
    slots, edge, _ = blocks.shape
    count_vectors = vec_blocks.shape[1]
    kernel = functools.partial(_tile_kernel, forward=forward)
    grid_spec = pltpu.PrefetchScalarGridSpec(
        num_scalar_prefetch=3,
        grid=(slots // GROUP,),
        in_specs=[
            pl.BlockSpec((GROUP, edge, edge), lambda g, *_: (g, 0, 0)),
            pl.BlockSpec(vec_blocks.shape, lambda g, *_: (0, 0, 0)),
        ],
        out_specs=pl.BlockSpec((out_blocks, count_vectors, edge), lambda g, *_: (0, 0, 0)),
    )
    return pl.pallas_call(
        kernel,
        grid_spec=grid_spec,
        out_shape=jax.ShapeDtypeStruct((out_blocks, count_vectors, edge), jnp.float32),
        compiler_params=pltpu.CompilerParams(dimension_semantics=("arbitrary",)),
        cost_estimate=pl.CostEstimate(
            flops=2 * slots * count_vectors * edge * edge,
            transcendentals=0,
            bytes_accessed=slots * edge * edge * 2 + out_blocks * count_vectors * edge * 4,
        ),
    )(slot_rows, columns, count, blocks, vec_blocks)


def _bits(n):
    bits = n.bit_length() - 1
    assert 1 << bits == n
    return bits


def gather_blocks(own, axis):
    n = lax.axis_size(axis)
    me = lax.axis_index(axis)
    buf = own[None]
    for b in reversed(range(_bits(n))):
        recv = lax.ppermute(buf, axis, [(i, i ^ (1 << b)) for i in range(n)])
        low = ((me >> b) & 1) == 0
        buf = jnp.where(low, jnp.stack([buf, recv], 1), jnp.stack([recv, buf], 1))
        buf = buf.reshape(-1, *own.shape)
    return buf.reshape(n * own.shape[0], *own.shape[1:])


def scatter_sum(x, axis, seg_blocks):
    n = lax.axis_size(axis)
    me = lax.axis_index(axis)
    buf = x.reshape(n, seg_blocks, *x.shape[1:])
    for b in range(_bits(n)):
        buf = buf.reshape(-1, 2, *buf.shape[1:])
        bit = (me >> b) & 1
        keep = lax.dynamic_index_in_dim(buf, bit, 1, keepdims=False)
        send = lax.dynamic_index_in_dim(buf, 1 - bit, 1, keepdims=False)
        buf = keep + lax.ppermute(send, axis, [(i, i ^ (1 << b)) for i in range(n)])
    return buf.reshape(seg_blocks, *x.shape[1:])


def body(vectors, blocks, row_ptr, col_idx):
    count_vectors = vectors.shape[0]
    segment = vectors.shape[1]
    tile_blocks = blocks[0]
    slots, edge, _ = tile_blocks.shape
    pointers = row_ptr[0]
    columns = col_idx[0]
    tile_rows = pointers.shape[0] - 1
    seg_blocks = segment // edge
    grid_rows = lax.axis_size("row")
    tile_cols = grid_rows * seg_blocks

    slot_ids = jnp.arange(slots, dtype=jnp.int32)
    slot_rows = jnp.sum((slot_ids[:, None] >= pointers[None, 1:]).astype(jnp.int32), axis=1)
    slot_rows = jnp.minimum(slot_rows, tile_rows - 1).astype(jnp.int32)
    columns = jnp.clip(columns, 0, tile_cols - 1).astype(jnp.int32)
    count = pointers[-1:].astype(jnp.int32)

    own = vectors.reshape(count_vectors, seg_blocks, edge).transpose(1, 0, 2)
    col_side = gather_blocks(own, "row")
    row_side = gather_blocks(own, "col")

    forward_sum = tile_apply(slot_rows, columns, count, tile_blocks, col_side, tile_rows, True)
    forward_part = scatter_sum(forward_sum, "col", seg_blocks)
    backward_sum = tile_apply(slot_rows, columns, count, tile_blocks, row_side, tile_cols, False)
    backward_part = scatter_sum(backward_sum, "row", seg_blocks)
    combined = forward_part + backward_part
    return combined.transpose(1, 0, 2).reshape(count_vectors, segment)


def solution(mesh):
    in_specs = (
        P(None, ("row", "col")),
        P("row", "col", None, None),
        P("row", "col"),
        P("row", "col"),
    )
    out_specs = P(None, ("row", "col"))
    return jax.shard_map(body, mesh=mesh, in_specs=in_specs, out_specs=out_specs, check_vma=False)
```

```python
import functools

import jax
import jax.numpy as jnp
from jax import lax
from jax.experimental import pallas as pl
from jax.experimental.pallas import tpu as pltpu
from jax.sharding import PartitionSpec as P

GROUP = 64


def _tile_kernel(rows_ref, cols_ref, count_ref, blocks_ref, vec_ref, out_ref, *, forward):
    g = pl.program_id(0)

    @pl.when(g == 0)
    def _():
        out_ref[...] = jnp.zeros_like(out_ref)

    count = count_ref[0]
    parts = []
    for t in range(GROUP):
        s = g * GROUP + t
        blk = blocks_ref[t]
        if forward:
            part = lax.dot_general(
                vec_ref[cols_ref[s]], blk, (((1,), (1,)), ((), ())),
                preferred_element_type=jnp.float32,
            )
        else:
            part = jnp.dot(vec_ref[rows_ref[s]], blk, preferred_element_type=jnp.float32)
        parts.append(jnp.where(s < count, part, jnp.zeros_like(part)))
    for t in range(GROUP):
        s = g * GROUP + t
        target = rows_ref[s] if forward else cols_ref[s]
        out_ref[target] += parts[t]


def tile_apply(slot_rows, columns, count, blocks, vec_blocks, out_blocks, forward):
    slots, edge, _ = blocks.shape
    count_vectors = vec_blocks.shape[1]
    kernel = functools.partial(_tile_kernel, forward=forward)
    grid_spec = pltpu.PrefetchScalarGridSpec(
        num_scalar_prefetch=3,
        grid=(slots // GROUP,),
        in_specs=[
            pl.BlockSpec((GROUP, edge, edge), lambda g, *_: (g, 0, 0)),
            pl.BlockSpec(vec_blocks.shape, lambda g, *_: (0, 0, 0)),
        ],
        out_specs=pl.BlockSpec((out_blocks, count_vectors, edge), lambda g, *_: (0, 0, 0)),
    )
    return pl.pallas_call(
        kernel,
        grid_spec=grid_spec,
        out_shape=jax.ShapeDtypeStruct((out_blocks, count_vectors, edge), jnp.float32),
        compiler_params=pltpu.CompilerParams(dimension_semantics=("arbitrary",)),
        cost_estimate=pl.CostEstimate(
            flops=2 * slots * count_vectors * edge * edge,
            transcendentals=0,
            bytes_accessed=slots * edge * edge * 2 + out_blocks * count_vectors * edge * 4,
        ),
    )(slot_rows, columns, count, blocks, vec_blocks)


def _bits(n):
    bits = n.bit_length() - 1
    assert 1 << bits == n
    return bits


def gather_blocks(own, axis):
    n = lax.axis_size(axis)
    me = lax.axis_index(axis)
    buf = own[None]
    for b in reversed(range(_bits(n))):
        recv = lax.ppermute(buf, axis, [(i, i ^ (1 << b)) for i in range(n)])
        low = ((me >> b) & 1) == 0
        buf = jnp.where(low, jnp.stack([buf, recv], 1), jnp.stack([recv, buf], 1))
        buf = buf.reshape(-1, *own.shape)
    return buf.reshape(n * own.shape[0], *own.shape[1:])


def scatter_sum(x, axis, seg_blocks):
    n = lax.axis_size(axis)
    me = lax.axis_index(axis)
    buf = x.reshape(n, seg_blocks, *x.shape[1:])
    for b in range(_bits(n)):
        buf = buf.reshape(-1, 2, *buf.shape[1:])
        bit = (me >> b) & 1
        keep = lax.dynamic_index_in_dim(buf, bit, 1, keepdims=False)
        send = lax.dynamic_index_in_dim(buf, 1 - bit, 1, keepdims=False)
        buf = keep + lax.ppermute(send, axis, [(i, i ^ (1 << b)) for i in range(n)])
    return buf.reshape(seg_blocks, *x.shape[1:])


def body(vectors, blocks, row_ptr, col_idx):
    count_vectors = vectors.shape[0]
    segment = vectors.shape[1]
    tile_blocks = blocks[0]
    slots, edge, _ = tile_blocks.shape
    pointers = row_ptr[0]
    columns = col_idx[0]
    tile_rows = pointers.shape[0] - 1
    seg_blocks = segment // edge
    grid_rows = lax.axis_size("row")
    tile_cols = grid_rows * seg_blocks

    slot_ids = jnp.arange(slots, dtype=jnp.int32)
    slot_rows = jnp.sum((slot_ids[:, None] >= pointers[None, 1:]).astype(jnp.int32), axis=1)
    slot_rows = jnp.minimum(slot_rows, tile_rows - 1).astype(jnp.int32)
    columns = jnp.clip(columns, 0, tile_cols - 1).astype(jnp.int32)
    count = pointers[-1:].astype(jnp.int32)

    own = vectors.reshape(count_vectors, seg_blocks, edge).transpose(1, 0, 2)
    col_side = gather_blocks(own, "row")
    row_side = gather_blocks(own, "col")

    forward_sum = tile_apply(slot_rows, columns, count, tile_blocks, col_side, tile_rows, True)
    forward_part = scatter_sum(forward_sum, "col", seg_blocks)
    backward_sum = tile_apply(slot_rows, columns, count, tile_blocks, row_side, tile_cols, False)
    backward_part = scatter_sum(backward_sum, "row", seg_blocks)
    combined = forward_part + backward_part
    return combined.transpose(1, 0, 2).reshape(count_vectors, segment)


def solution(mesh):
    in_specs = (
        P(None, ("row", "col")),
        P("row", "col", None, None),
        P("row", "col"),
        P("row", "col"),
    )
    out_specs = P(None, ("row", "col"))
    return jax.shard_map(body, mesh=mesh, in_specs=in_specs, out_specs=out_specs, check_vma=False)
```

```python
import functools

import jax
import jax.numpy as jnp
from jax import lax
from jax.experimental import pallas as pl
from jax.experimental.pallas import tpu as pltpu
from jax.sharding import PartitionSpec as P

GROUP = 96


def _tile_kernel(rows_ref, cols_ref, count_ref, blocks_ref, vec_ref, out_ref, *, forward):
    g = pl.program_id(0)

    @pl.when(g == 0)
    def _():
        out_ref[...] = jnp.zeros_like(out_ref)

    count = count_ref[count_ref.shape[0] - 1]
    parts = []
    for t in range(GROUP):
        s = g * GROUP + t
        blk = blocks_ref[t]
        if forward:
            part = lax.dot_general(
                vec_ref[cols_ref[s]], blk, (((1,), (1,)), ((), ())),
                preferred_element_type=jnp.float32,
            )
        else:
            part = jnp.dot(vec_ref[rows_ref[s]], blk, preferred_element_type=jnp.float32)
        parts.append(jnp.where(s < count, part, jnp.zeros_like(part)))
    for t in range(GROUP):
        s = g * GROUP + t
        target = rows_ref[s] if forward else cols_ref[s]
        out_ref[target] += parts[t]


def tile_apply(slot_rows, columns, count, blocks, vec_blocks, out_blocks, forward):
    slots, edge, _ = blocks.shape
    count_vectors = vec_blocks.shape[1]
    kernel = functools.partial(_tile_kernel, forward=forward)
    grid_spec = pltpu.PrefetchScalarGridSpec(
        num_scalar_prefetch=3,
        grid=(slots // GROUP,),
        in_specs=[
            pl.BlockSpec((GROUP, edge, edge), lambda g, *_: (g, 0, 0)),
            pl.BlockSpec(vec_blocks.shape, lambda g, *_: (0, 0, 0)),
        ],
        out_specs=pl.BlockSpec((out_blocks, count_vectors, edge), lambda g, *_: (0, 0, 0)),
    )
    return pl.pallas_call(
        kernel,
        grid_spec=grid_spec,
        out_shape=jax.ShapeDtypeStruct((out_blocks, count_vectors, edge), jnp.float32),
        compiler_params=pltpu.CompilerParams(dimension_semantics=("arbitrary",)),
        cost_estimate=pl.CostEstimate(
            flops=2 * slots * count_vectors * edge * edge,
            transcendentals=0,
            bytes_accessed=slots * edge * edge * 2 + out_blocks * count_vectors * edge * 4,
        ),
    )(slot_rows, columns, count, blocks, vec_blocks)


def _bits(n):
    bits = n.bit_length() - 1
    assert 1 << bits == n
    return bits


def gather_blocks(own, axis):
    n = lax.axis_size(axis)
    me = lax.axis_index(axis)
    buf = own[None]
    for b in reversed(range(_bits(n))):
        recv = lax.ppermute(buf, axis, [(i, i ^ (1 << b)) for i in range(n)])
        low = ((me >> b) & 1) == 0
        buf = jnp.where(low, jnp.stack([buf, recv], 1), jnp.stack([recv, buf], 1))
        buf = buf.reshape(-1, *own.shape)
    return buf.reshape(n * own.shape[0], *own.shape[1:])


def scatter_sum(x, axis, seg_blocks):
    n = lax.axis_size(axis)
    me = lax.axis_index(axis)
    buf = x.reshape(n, seg_blocks, *x.shape[1:])
    for b in range(_bits(n)):
        buf = buf.reshape(-1, 2, *buf.shape[1:])
        bit = (me >> b) & 1
        keep = lax.dynamic_index_in_dim(buf, bit, 1, keepdims=False)
        send = lax.dynamic_index_in_dim(buf, 1 - bit, 1, keepdims=False)
        buf = keep + lax.ppermute(send, axis, [(i, i ^ (1 << b)) for i in range(n)])
    return buf.reshape(seg_blocks, *x.shape[1:])


def body(vectors, blocks, row_ptr, col_idx):
    count_vectors = vectors.shape[0]
    segment = vectors.shape[1]
    tile_blocks = blocks[0]
    slots, edge, _ = tile_blocks.shape
    pointers = row_ptr[0]
    columns = col_idx[0]
    tile_rows = pointers.shape[0] - 1
    seg_blocks = segment // edge
    grid_rows = lax.axis_size("row")
    tile_cols = grid_rows * seg_blocks

    slot_ids = jnp.arange(slots, dtype=jnp.int32)
    slot_rows = jnp.sum((slot_ids[:, None] >= pointers[None, :]).astype(jnp.int32), axis=1)
    slot_rows = jnp.minimum(slot_rows - 1, tile_rows - 1).astype(jnp.int32)
    columns = columns.astype(jnp.int32)
    count = pointers.astype(jnp.int32)

    own = vectors.reshape(count_vectors, seg_blocks, edge).transpose(1, 0, 2)
    col_side = gather_blocks(own, "row")
    row_side = gather_blocks(own, "col")

    forward_sum = tile_apply(slot_rows, columns, count, tile_blocks, col_side, tile_rows, True)
    forward_part = scatter_sum(forward_sum, "col", seg_blocks)
    backward_sum = tile_apply(slot_rows, columns, count, tile_blocks, row_side, tile_cols, False)
    backward_part = scatter_sum(backward_sum, "row", seg_blocks)
    combined = forward_part + backward_part
    return combined.transpose(1, 0, 2).reshape(count_vectors, segment)


def solution(mesh):
    in_specs = (
        P(None, ("row", "col")),
        P("row", "col", None, None),
        P("row", "col"),
        P("row", "col"),
    )
    out_specs = P(None, ("row", "col"))
    return jax.shard_map(body, mesh=mesh, in_specs=in_specs, out_specs=out_specs, check_vma=False)
```

```python
import functools

import jax
import jax.numpy as jnp
from jax import lax
from jax.experimental import pallas as pl
from jax.experimental.pallas import tpu as pltpu
from jax.sharding import PartitionSpec as P

GROUP = 96


def _tile_kernel(rows_ref, cols_ref, count_ref, blocks_ref, vec_ref, out_ref, *, forward):
    g = pl.program_id(0)

    @pl.when(g == 0)
    def _():
        out_ref[...] = jnp.zeros_like(out_ref)

    count = count_ref[count_ref.shape[0] - 1]
    parts = []
    for t in range(GROUP):
        s = g * GROUP + t
        blk = blocks_ref[t]
        if forward:
            part = lax.dot_general(
                vec_ref[cols_ref[s]], blk, (((1,), (1,)), ((), ())),
                preferred_element_type=jnp.float32,
            )
        else:
            part = jnp.dot(vec_ref[rows_ref[s]], blk, preferred_element_type=jnp.float32)
        parts.append(jnp.where(s < count, part, jnp.zeros_like(part)))
    for t in range(GROUP):
        s = g * GROUP + t
        target = rows_ref[s] if forward else cols_ref[s]
        out_ref[target] += parts[t]


def tile_apply(slot_rows, columns, count, blocks, vec_blocks, out_blocks, forward):
    slots, edge, _ = blocks.shape
    count_vectors = vec_blocks.shape[1]
    kernel = functools.partial(_tile_kernel, forward=forward)
    grid_spec = pltpu.PrefetchScalarGridSpec(
        num_scalar_prefetch=3,
        grid=(slots // GROUP,),
        in_specs=[
            pl.BlockSpec((GROUP, edge, edge), lambda g, *_: (g, 0, 0)),
            pl.BlockSpec(vec_blocks.shape, lambda g, *_: (0, 0, 0)),
        ],
        out_specs=pl.BlockSpec((out_blocks, count_vectors, edge), lambda g, *_: (0, 0, 0)),
    )
    return pl.pallas_call(
        kernel,
        grid_spec=grid_spec,
        out_shape=jax.ShapeDtypeStruct((out_blocks, count_vectors, edge), jnp.float32),
        compiler_params=pltpu.CompilerParams(dimension_semantics=("arbitrary",)),
        cost_estimate=pl.CostEstimate(
            flops=2 * slots * count_vectors * edge * edge,
            transcendentals=0,
            bytes_accessed=slots * edge * edge * 2 + out_blocks * count_vectors * edge * 4,
        ),
    )(slot_rows, columns, count, blocks, vec_blocks)


def _bits(n):
    bits = n.bit_length() - 1
    assert 1 << bits == n
    return bits


def gather_blocks(own, axis):
    n = lax.axis_size(axis)
    me = lax.axis_index(axis)
    buf = own[None]
    for b in reversed(range(_bits(n))):
        recv = lax.ppermute(buf, axis, [(i, i ^ (1 << b)) for i in range(n)])
        low = ((me >> b) & 1) == 0
        buf = jnp.where(low, jnp.stack([buf, recv], 1), jnp.stack([recv, buf], 1))
        buf = buf.reshape(-1, *own.shape)
    return buf.reshape(n * own.shape[0], *own.shape[1:])


def scatter_sum(x, axis, seg_blocks):
    n = lax.axis_size(axis)
    me = lax.axis_index(axis)
    buf = x.reshape(n, seg_blocks, *x.shape[1:])
    for b in range(_bits(n)):
        buf = buf.reshape(-1, 2, *buf.shape[1:])
        bit = (me >> b) & 1
        keep = lax.dynamic_index_in_dim(buf, bit, 1, keepdims=False)
        send = lax.dynamic_index_in_dim(buf, 1 - bit, 1, keepdims=False)
        buf = keep + lax.ppermute(send, axis, [(i, i ^ (1 << b)) for i in range(n)])
    return buf.reshape(seg_blocks, *x.shape[1:])


def scatter_a2a(x, axis, seg_blocks):
    n = lax.axis_size(axis)
    y = lax.all_to_all(x, axis, 0, 0, tiled=True)
    return y.reshape(n, seg_blocks, *x.shape[1:]).sum(0)


def gather_a2a(own, axis):
    n = lax.axis_size(axis)
    y = jnp.broadcast_to(own[None], (n,) + own.shape).reshape(n * own.shape[0], *own.shape[1:])
    return lax.all_to_all(y, axis, 0, 0, tiled=True)


def body(vectors, blocks, row_ptr, col_idx):
    count_vectors = vectors.shape[0]
    segment = vectors.shape[1]
    tile_blocks = blocks[0]
    slots, edge, _ = tile_blocks.shape
    pointers = row_ptr[0]
    columns = col_idx[0]
    tile_rows = pointers.shape[0] - 1
    seg_blocks = segment // edge
    grid_rows = lax.axis_size("row")
    tile_cols = grid_rows * seg_blocks

    slot_ids = jnp.arange(slots, dtype=jnp.int32)
    slot_rows = jnp.sum((slot_ids[:, None] >= pointers[None, :]).astype(jnp.int32), axis=1)
    slot_rows = jnp.minimum(slot_rows - 1, tile_rows - 1).astype(jnp.int32)
    columns = columns.astype(jnp.int32)
    count = pointers.astype(jnp.int32)

    own = vectors.reshape(count_vectors, seg_blocks, edge).transpose(1, 0, 2)
    col_side = gather_blocks(own, "row")
    row_side = gather_blocks(own, "col")

    forward_sum = tile_apply(slot_rows, columns, count, tile_blocks, col_side, tile_rows, True)
    forward_part = scatter_sum(forward_sum, "col", seg_blocks)
    backward_sum = tile_apply(slot_rows, columns, count, tile_blocks, row_side, tile_cols, False)
    backward_part = scatter_a2a(backward_sum, "row", seg_blocks)
    combined = forward_part + backward_part
    return combined.transpose(1, 0, 2).reshape(count_vectors, segment)


def solution(mesh):
    in_specs = (
        P(None, ("row", "col")),
        P("row", "col", None, None),
        P("row", "col"),
        P("row", "col"),
    )
    out_specs = P(None, ("row", "col"))
    return jax.shard_map(body, mesh=mesh, in_specs=in_specs, out_specs=out_specs, check_vma=False)
```

```python
import functools

import jax
import jax.numpy as jnp
from jax import lax
from jax.experimental import pallas as pl
from jax.experimental.pallas import tpu as pltpu
from jax.sharding import PartitionSpec as P


GROUP = 96


def _tile_kernel(rows_ref, cols_ref, count_ref, blocks_ref, vec_ref, out_ref, *, forward):
    g = pl.program_id(0)

    @pl.when(g == 0)
    def _():
        out_ref[...] = jnp.zeros_like(out_ref)

    count = count_ref[count_ref.shape[0] - 1]
    parts = []
    for t in range(GROUP):
        s = g * GROUP + t
        blk = blocks_ref[t]
        if forward:
            part = lax.dot_general(
                vec_ref[cols_ref[s]], blk, (((1,), (1,)), ((), ())),
                preferred_element_type=jnp.float32,
            )
        else:
            part = jnp.dot(vec_ref[rows_ref[s]], blk, preferred_element_type=jnp.float32)
        parts.append(jnp.where(s < count, part, jnp.zeros_like(part)))
    for t in range(GROUP):
        s = g * GROUP + t
        target = rows_ref[s] if forward else cols_ref[s]
        out_ref[target] += parts[t]


def tile_apply(slot_rows, columns, count, blocks, vec_blocks, out_blocks, forward):
    slots, edge, _ = blocks.shape
    count_vectors = vec_blocks.shape[1]
    kernel = functools.partial(_tile_kernel, forward=forward)
    grid_spec = pltpu.PrefetchScalarGridSpec(
        num_scalar_prefetch=3,
        grid=(slots // GROUP,),
        in_specs=[
            pl.BlockSpec((GROUP, edge, edge), lambda g, *_: (g, 0, 0)),
            pl.BlockSpec(vec_blocks.shape, lambda g, *_: (0, 0, 0)),
        ],
        out_specs=pl.BlockSpec((out_blocks, count_vectors, edge), lambda g, *_: (0, 0, 0)),
    )
    return pl.pallas_call(
        kernel,
        grid_spec=grid_spec,
        out_shape=jax.ShapeDtypeStruct((out_blocks, count_vectors, edge), jnp.float32),
        compiler_params=pltpu.CompilerParams(dimension_semantics=("arbitrary",)),
        cost_estimate=pl.CostEstimate(
            flops=2 * slots * count_vectors * edge * edge,
            transcendentals=0,
            bytes_accessed=slots * edge * edge * 2 + out_blocks * count_vectors * edge * 4,
        ),
    )(slot_rows, columns, count, blocks, vec_blocks)


def _bits(n):
    bits = n.bit_length() - 1
    assert 1 << bits == n
    return bits


def gather_blocks(own, axis, labels):
    n = lax.axis_size(axis)
    back = {lab: i for i, lab in enumerate(labels)}
    label = jnp.asarray(labels, jnp.int32)[lax.axis_index(axis)]
    buf = own[None]
    for b in reversed(range(_bits(n))):
        pairs = [(i, back[labels[i] ^ (1 << b)]) for i in range(n)]
        recv = lax.ppermute(buf, axis, pairs)
        low = ((label >> b) & 1) == 0
        buf = jnp.where(low, jnp.stack([buf, recv], 1), jnp.stack([recv, buf], 1))
        buf = buf.reshape(-1, *own.shape)
    return buf.reshape(n * own.shape[0], *own.shape[1:])


def scatter_sum(x, axis, seg_blocks, labels):
    n = lax.axis_size(axis)
    back = {lab: i for i, lab in enumerate(labels)}
    label = jnp.asarray(labels, jnp.int32)[lax.axis_index(axis)]
    buf = x.reshape(n, seg_blocks, *x.shape[1:])
    for b in range(_bits(n)):
        buf = buf.reshape(-1, 2, *buf.shape[1:])
        bit = (label >> b) & 1
        keep = lax.dynamic_index_in_dim(buf, bit, 1, keepdims=False)
        send = lax.dynamic_index_in_dim(buf, 1 - bit, 1, keepdims=False)
        pairs = [(i, back[labels[i] ^ (1 << b)]) for i in range(n)]
        buf = keep + lax.ppermute(send, axis, pairs)
    return buf.reshape(seg_blocks, *x.shape[1:])


def col_labels(n):
    ring = (0, 1, 2, 3, 6, 7, 4, 5)
    if n != 32:
        return list(range(n))
    return [(c // 16) * 16 + ring[(c // 2) % 8] * 2 + c % 2 for c in range(n)]


def scatter_a2a(x, axis, seg_blocks):
    n = lax.axis_size(axis)
    y = lax.all_to_all(x, axis, 0, 0, tiled=True)
    return y.reshape(n, seg_blocks, *x.shape[1:]).sum(0)


def body(vectors, blocks, row_ptr, col_idx):
    count_vectors = vectors.shape[0]
    segment = vectors.shape[1]
    tile_blocks = blocks[0]
    slots, edge, _ = tile_blocks.shape
    pointers = row_ptr[0]
    columns = col_idx[0]
    tile_rows = pointers.shape[0] - 1
    seg_blocks = segment // edge
    grid_rows = lax.axis_size("row")
    tile_cols = grid_rows * seg_blocks

    slot_ids = jnp.arange(slots, dtype=jnp.int32)
    slot_rows = jnp.sum((slot_ids[:, None] >= pointers[None, :]).astype(jnp.int32), axis=1)
    slot_rows = jnp.minimum(slot_rows - 1, tile_rows - 1).astype(jnp.int32)
    columns = columns.astype(jnp.int32)
    count = pointers.astype(jnp.int32)

    own = vectors.reshape(count_vectors, seg_blocks, edge).transpose(1, 0, 2)
    labels = col_labels(lax.axis_size("col"))
    placed = jnp.asarray(
        [labels[i // seg_blocks] * seg_blocks + i % seg_blocks for i in range(tile_rows)], jnp.int32
    )
    slot_rows = placed[slot_rows]
    col_side = gather_blocks(own, "row", list(range(grid_rows)))
    row_side = gather_blocks(own, "col", labels)

    forward_sum = tile_apply(slot_rows, columns, count, tile_blocks, col_side, tile_rows, True)
    forward_part = scatter_sum(forward_sum, "col", seg_blocks, labels)
    backward_sum = tile_apply(slot_rows, columns, count, tile_blocks, row_side, tile_cols, False)
    backward_part = scatter_a2a(backward_sum, "row", seg_blocks)
    combined = forward_part + backward_part
    return combined.transpose(1, 0, 2).reshape(count_vectors, segment)


def solution(mesh):
    in_specs = (
        P(None, ("row", "col")),
        P("row", "col", None, None),
        P("row", "col"),
        P("row", "col"),
    )
    out_specs = P(None, ("row", "col"))

    return jax.shard_map(body, mesh=mesh, in_specs=in_specs, out_specs=out_specs, check_vma=False)
```
